128 devices in a mesh: row: 8 (over y, core), col: 16 (over x, z).
Axes of the slice: x: 4, y: 4, z: 4, core: 2. Of those that a mesh axis runs over, the one named last changes fastest.
Arguments:
- source_mass: float32 [64, 16, 1024], P('row', None, 'col'), may hold values from 0.3 to 3
- target_mass: float32 [64, 16, 1024], P('col', None, 'row'), may hold values from 0.3 to 3
- tile_list: int32 [8, 16, 8, 2], P('row', 'col'), may hold values from 0 to 63, as said below
- kernel_tiles: bfloat16 [8, 16, 8, 1024, 1024], P('row', 'col'), may hold values from 0.001 to 1
Outputs:
- log_u: float32 [64, 16, 1024], P('row', None, 'col')
- log_v: float32 [64, 16, 1024], P('col', None, 'row')
The draws below stay inside these ranges and needn't reach their ends.
Inputs may be any that keep to these rules, and one draw needn't show every extreme that they name: `tile_list`: device (i, j) holds 8 distinct tiles whose block rows lie in i * 8 to (i + 1) * 8 - 1 and block columns in j * 4 to (j + 1) * 4 - 1; every block row and every block column has at least one tile; the number of tiles of a block row varies.
All inputs are finite; a program needn't handle non-finite values.
Results may differ from the reference program's by a relative error of at most 0.0003.
Values may be sent and summed in bfloat16 or wider, within the bound.
No kernel may reach another device: no remote copies, remote signals or barrier semaphores. Data moves between devices by JAX's collectives and lax.ppermute only.
A program may use at most 128 MiB of HBM per device.

```python
import math
import jax
import jax.numpy as jnp
from jax import lax

B = 1024
COLS = 16
ITERS = 2
RB_DEV = 8
CB_DEV = 4
TILES_DEV = 8
NBR = 64
NBC = 64
N_ROW = 8
N_COL = 16


def tile_plan(key):
    base = jax.random.fold_in(key, 5)
    slots = RB_DEV * CB_DEV

    def one_device(device):
        row_index = device // N_COL
        col_index = device % N_COL
        local_key = jax.random.fold_in(base, device)
        scores = jax.random.randint(local_key, (slots,), 0, 1 << 20) * slots + jnp.arange(slots, dtype=jnp.int32)
        forced = col_index % RB_DEV * CB_DEV + row_index % CB_DEV
        scores = scores + jnp.where(jnp.arange(slots, dtype=jnp.int32) == forced, 1 << 30, 0).astype(jnp.int32)
        top_scores, picked = lax.top_k(scores, TILES_DEV)
        rows_out = row_index * RB_DEV + picked // CB_DEV
        cols_out = col_index * CB_DEV + picked % CB_DEV
        return jnp.stack([rows_out, cols_out], axis=-1).astype(jnp.int32)
    plan = jax.vmap(one_device)(jnp.arange(N_ROW * N_COL, dtype=jnp.int32))
    return plan.reshape(N_ROW, N_COL, TILES_DEV, 2).astype(jnp.int32)


def draw_tile_list(key, part):
    return tile_plan(key)


def draw_kernel_tiles(key, part):
    plan = tile_plan(key)
    low_scale = 0.1
    sharpness = 500.0
    row_scale = jnp.exp(jax.random.uniform(jax.random.fold_in(key, 11), (NBR, B), jnp.float32, jnp.log(low_scale), 0.0))
    col_scale = jnp.exp(jax.random.uniform(jax.random.fold_in(key, 12), (NBC, B), jnp.float32, jnp.log(low_scale), 0.0))
    distance = jax.random.uniform(jax.random.fold_in(key, 13), (N_ROW, N_COL, TILES_DEV, B, B), jnp.float32, 0.0, 1.0)
    entries = jnp.exp(-sharpness * distance)
    row_part = row_scale[plan[..., 0]]
    col_part = col_scale[plan[..., 1]]
    values = jnp.clip(row_part[..., :, None] * col_part[..., None, :] * entries, 0.00105, 1.0)
    return values.astype(jnp.bfloat16)


def level_of(rng, shape, pieces, smallest, top_value):
    def one(dim, shards_of):
        heights = jax.random.uniform(jax.random.fold_in(jax.random.fold_in(rng, 6), dim), (shards_of,), jnp.float32, smallest / len(pieces), top_value / len(pieces))
        return jnp.repeat(jnp.exp(heights), shape[dim] // shards_of).reshape((-1,) + (1,) * (len(shape) - dim - 1))

    level = one(*pieces[0])
    for cut in pieces[1:]:
        level = level * one(*cut)
    return level


def setup_inputs(seed: int = 0) -> dict:
    key_of = jax.random.split(jax.random.key(seed), 5)
    return {
        "source_mass": jnp.clip(jnp.exp(math.log(3.0) - 2.3025851 * jax.random.uniform(key_of[0], (NBR, COLS, B), jnp.float32) ** level_of(key_of[0], (NBR, COLS, B), ((0, 8), (2, 16)), -0.2, 0.2)), 0.3, 3.0),
        "target_mass": jnp.clip(jnp.exp(math.log(3.0) - 2.3025851 * jax.random.uniform(key_of[1], (NBC, COLS, B), jnp.float32) ** level_of(key_of[1], (NBC, COLS, B), ((0, 16), (2, 8)), -0.2, 0.2)), 0.3, 3.0),
        "tile_list": draw_tile_list(jax.random.fold_in(key_of[4], 71), 0),
        "kernel_tiles": draw_kernel_tiles(jax.random.fold_in(key_of[4], 71), 0),
    }


def reference(source_mass, target_mass, tile_list, kernel_tiles):
    tiles = kernel_tiles.reshape(-1, B, B)
    block_rows = tile_list[..., 0].reshape(-1).astype(jnp.int32)
    block_cols = tile_list[..., 1].reshape(-1).astype(jnp.int32)
    target_b = jnp.ones((NBC, COLS, B), jnp.bfloat16)
    scale_u = jnp.zeros((NBR, COLS, B), jnp.float32)
    scale_v = jnp.zeros((NBC, COLS, B), jnp.float32)
    for step in range(ITERS):
        def forward(carry, item):
            tile, brow, bcol = item
            block = lax.dynamic_index_in_dim(target_b, bcol, 0, keepdims=False)
            prod = lax.dot_general(block, tile, (((1,), (1,)), ((), ())), preferred_element_type=jnp.float32)
            return carry.at[brow].add(prod), None

        row_sum, _ = lax.scan(forward, jnp.zeros((NBR, COLS, B), jnp.float32), (tiles, block_rows, block_cols))
        scale_u = source_mass / row_sum
        source_b = scale_u.astype(jnp.bfloat16)

        def backward(carry, item):
            tile, brow, bcol = item
            block = lax.dynamic_index_in_dim(source_b, brow, 0, keepdims=False)
            prod = lax.dot_general(block, tile, (((1,), (0,)), ((), ())), preferred_element_type=jnp.float32)
            return carry.at[bcol].add(prod), None

        col_sum, _ = lax.scan(backward, jnp.zeros((NBC, COLS, B), jnp.float32), (tiles, block_rows, block_cols))
        scale_v = target_mass / col_sum
        target_b = scale_v.astype(jnp.bfloat16)
    return jnp.log(scale_u), jnp.log(scale_v)
```

```python
import jax
import jax.numpy as jnp
from jax import lax
from jax.sharding import PartitionSpec as P

ITERS = 2


def collect(selector, count, values):
    onehot = (selector[None, :] == jnp.arange(count, dtype=jnp.int32)[:, None]).astype(jnp.float32)
    return jnp.einsum("rt,tcp->rcp", onehot, values, precision=lax.Precision.HIGHEST)


def forward_terms(tiles, target_full, col_local, row_local, count):
    picked = target_full[col_local]
    products = jnp.einsum("tcq,tpq->tcp", picked, tiles, preferred_element_type=jnp.float32)
    return collect(row_local, count, products)


def backward_terms(tiles, source_full, row_local, col_local, count):
    picked = source_full[row_local]
    products = jnp.einsum("tcp,tpq->tcq", picked, tiles, preferred_element_type=jnp.float32)
    return collect(col_local, count, products)


def reduce_scatter(values, axis, parts):
    lead = values.shape[:-1]
    width = values.shape[-1] // parts
    split = values.reshape(lead + (parts, width))
    moved = lax.all_to_all(split, axis, len(lead), len(lead), tiled=True)
    return moved.sum(axis=len(lead))


def body(source_mass, target_mass, tile_list, kernel_tiles):
    width = kernel_tiles.shape[-1]
    tiles = kernel_tiles.reshape(-1, width, width)
    listed = tile_list.reshape(-1, 2)
    row_count = source_mass.shape[0]
    col_count = target_mass.shape[0]
    columns = source_mass.shape[1]
    n_col = width // source_mass.shape[2]
    n_row = width // target_mass.shape[2]
    row_local = listed[:, 0] - lax.axis_index("row") * row_count
    col_local = listed[:, 1] - lax.axis_index("col") * col_count
    target_full = jnp.ones((col_count, columns, width), jnp.bfloat16)
    scale_u = source_mass
    scale_v = target_mass
    for step in range(ITERS):
        if step > 0:
            target_full = lax.all_gather(scale_v.astype(jnp.bfloat16), "row", axis=2, tiled=True)
        row_sums = reduce_scatter(
            forward_terms(tiles, target_full, col_local, row_local, row_count), "col", n_col
        )
        scale_u = source_mass / row_sums
        source_full = lax.all_gather(scale_u.astype(jnp.bfloat16), "col", axis=2, tiled=True)
        col_sums = reduce_scatter(
            backward_terms(tiles, source_full, row_local, col_local, col_count), "row", n_row
        )
        scale_v = target_mass / col_sums
    log_u = jnp.log(scale_u)
    log_v = jnp.log(scale_v)
    return (log_u, log_v)


def solution(mesh):
    placed = (
        P("row", None, "col"),
        P("col", None, "row"),
        P("row", "col", None, None),
        P("row", "col", None, None, None),
    )
    return jax.shard_map(
        body,
        mesh=mesh,
        in_specs=placed,
        out_specs=(P("row", None, "col"), P("col", None, "row")),
        check_vma=False,
    )
```

```python
import jax
import jax.numpy as jnp
from jax import lax
from jax.sharding import PartitionSpec as P

ITERS = 2


def collect(selector, count, values):
    onehot = (selector[None, :] == jnp.arange(count, dtype=jnp.int32)[:, None]).astype(jnp.float32)
    return jnp.einsum("rt,tcp->rcp", onehot, values, precision=lax.Precision.HIGHEST)


def forward_terms(tiles, target_full, col_local, row_local, count):
    picked = target_full[col_local]
    products = jnp.einsum("tcq,tpq->tcp", picked, tiles, preferred_element_type=jnp.float32)
    return collect(row_local, count, products)


def backward_terms(tiles, source_full, row_local, col_local, count):
    picked = source_full[row_local]
    products = jnp.einsum("tcp,tpq->tcq", picked, tiles, preferred_element_type=jnp.float32)
    return collect(col_local, count, products)


def reduce_scatter(values, axis, parts):
    lead = values.shape[:-1]
    width = values.shape[-1] // parts
    split = values.reshape(lead + (parts, width))
    moved = lax.all_to_all(split, axis, len(lead), len(lead), tiled=True)
    return moved.sum(axis=len(lead))


def all_gather(values, axis, parts):
    copies = jnp.broadcast_to(values[None], (parts,) + values.shape)
    moved = lax.all_to_all(copies, axis, 0, 0, tiled=True)
    lead = values.shape[:-1]
    return jnp.moveaxis(moved, 0, -2).reshape(lead + (parts * values.shape[-1],))


def body(source_mass, target_mass, tile_list, kernel_tiles):
    width = kernel_tiles.shape[-1]
    tiles = kernel_tiles.reshape(-1, width, width)
    listed = tile_list.reshape(-1, 2)
    row_count = source_mass.shape[0]
    col_count = target_mass.shape[0]
    columns = source_mass.shape[1]
    n_col = width // source_mass.shape[2]
    n_row = width // target_mass.shape[2]
    row_local = listed[:, 0] - lax.axis_index("row") * row_count
    col_local = listed[:, 1] - lax.axis_index("col") * col_count
    target_full = jnp.ones((col_count, columns, width), jnp.bfloat16)
    scale_u = source_mass
    scale_v = target_mass
    for step in range(ITERS):
        if step > 0:
            target_full = all_gather(scale_v.astype(jnp.bfloat16), "row", n_row)
        row_sums = reduce_scatter(
            forward_terms(tiles, target_full, col_local, row_local, row_count), "col", n_col
        )
        scale_u = source_mass / row_sums
        source_full = all_gather(scale_u.astype(jnp.bfloat16), "col", n_col)
        col_sums = reduce_scatter(
            backward_terms(tiles, source_full, row_local, col_local, col_count), "row", n_row
        )
        scale_v = target_mass / col_sums
    log_u = jnp.log(scale_u)
    log_v = jnp.log(scale_v)
    return (log_u, log_v)


def solution(mesh):
    placed = (
        P("row", None, "col"),
        P("col", None, "row"),
        P("row", "col", None, None),
        P("row", "col", None, None, None),
    )
    return jax.shard_map(
        body,
        mesh=mesh,
        in_specs=placed,
        out_specs=(P("row", None, "col"), P("col", None, "row")),
        check_vma=False,
    )
```

```python
import jax
import jax.numpy as jnp
from jax import lax
from jax.sharding import PartitionSpec as P

ITERS = 2


def collect(selector, count, values):
    onehot = (selector[None, :] == jnp.arange(count, dtype=jnp.int32)[:, None]).astype(jnp.float32)
    return jnp.einsum("rt,tcp->rcp", onehot, values, precision=lax.Precision.HIGHEST)


def forward_terms(tiles, target_full, col_local, row_local, count):
    picked = target_full[col_local]
    products = jnp.einsum("tcq,tpq->tcp", picked, tiles, preferred_element_type=jnp.float32)
    return collect(row_local, count, products)


def backward_terms(tiles, source_full, row_local, col_local, count):
    picked = source_full[row_local]
    products = jnp.einsum("tcp,tpq->tcq", picked, tiles, preferred_element_type=jnp.float32)
    return collect(col_local, count, products)


def reduce_scatter(values, axis, parts):
    lead = values.shape[:-1]
    width = values.shape[-1] // parts
    split = values.reshape(lead + (parts, width))
    moved = lax.all_to_all(split, axis, len(lead), len(lead), tiled=True)
    return moved.sum(axis=len(lead))


def all_gather(values, axis, parts):
    copies = jnp.broadcast_to(values[None], (parts,) + values.shape)
    moved = lax.all_to_all(copies, axis, 0, 0, tiled=True)
    lead = values.shape[:-1]
    return jnp.moveaxis(moved, 0, -2).reshape(lead + (parts * values.shape[-1],))


def body(source_mass, target_mass, tile_list, kernel_tiles):
    width = kernel_tiles.shape[-1]
    tiles = kernel_tiles.reshape(-1, width, width)
    listed = tile_list.reshape(-1, 2)
    row_count = source_mass.shape[0]
    col_count = target_mass.shape[0]
    columns = source_mass.shape[1]
    n_col = width // source_mass.shape[2]
    n_row = width // target_mass.shape[2]
    row_local = listed[:, 0] - lax.axis_index("row") * row_count
    col_local = listed[:, 1] - lax.axis_index("col") * col_count
    row_part = collect(row_local, row_count, tiles.sum(axis=2, dtype=jnp.float32)[:, None, :])[:, 0, :]
    payload = jnp.concatenate([source_mass.reshape(-1), row_part.reshape(-1)])
    copies = jnp.broadcast_to(payload[None], (n_col,) + payload.shape)
    moved = lax.all_to_all(copies, "col", 0, 0, tiled=True)
    split = source_mass.size
    mass_full = jnp.moveaxis(moved[:, :split].reshape((n_col,) + source_mass.shape), 0, 2)
    mass_full = mass_full.reshape(row_count, columns, width)
    row_full = moved[:, split:].reshape(n_col, row_count, width).sum(axis=0)
    source_full = (mass_full / row_full[:, None, :]).astype(jnp.bfloat16)
    col_sums = reduce_scatter(
        backward_terms(tiles, source_full, row_local, col_local, col_count), "row", n_row
    )
    scale_v = target_mass / col_sums
    for step in range(1, ITERS):
        target_full = all_gather(scale_v.astype(jnp.bfloat16), "row", n_row)
        row_sums = reduce_scatter(
            forward_terms(tiles, target_full, col_local, row_local, row_count), "col", n_col
        )
        scale_u = source_mass / row_sums
        source_full = all_gather(scale_u.astype(jnp.bfloat16), "col", n_col)
        col_sums = reduce_scatter(
            backward_terms(tiles, source_full, row_local, col_local, col_count), "row", n_row
        )
        scale_v = target_mass / col_sums
    log_u = jnp.log(scale_u)
    log_v = jnp.log(scale_v)
    return (log_u, log_v)


def solution(mesh):
    placed = (
        P("row", None, "col"),
        P("col", None, "row"),
        P("row", "col", None, None),
        P("row", "col", None, None, None),
    )
    return jax.shard_map(
        body,
        mesh=mesh,
        in_specs=placed,
        out_specs=(P("row", None, "col"), P("col", None, "row")),
        check_vma=False,
    )
```

```python
import jax
import jax.numpy as jnp
from jax import lax
from jax.sharding import PartitionSpec as P

ITERS = 2


def collect(selector, count, values):
    onehot = (selector[None, :] == jnp.arange(count, dtype=jnp.int32)[:, None]).astype(jnp.float32)
    return jnp.einsum("rt,tcp->rcp", onehot, values, precision=lax.Precision.HIGHEST)


def forward_terms(tiles, target_full, col_local, row_local, count):
    picked = target_full[col_local]
    products = jnp.einsum("tcq,tpq->tcp", picked, tiles, preferred_element_type=jnp.float32)
    return collect(row_local, count, products)


def backward_terms(tiles, source_full, row_local, col_local, count):
    picked = source_full[row_local]
    products = jnp.einsum("tcp,tpq->tcq", picked, tiles, preferred_element_type=jnp.float32)
    return collect(col_local, count, products)


LANES = 128


def reduce_scatter(values, axis, parts):
    lead = values.shape[:-1]
    width = values.shape[-1] // parts
    split = jnp.moveaxis(values.reshape(lead + (parts, width)), -2, 0)
    dense = split.reshape(parts, -1, LANES)
    moved = lax.all_to_all(dense, axis, 0, 0, tiled=True)
    return moved.sum(axis=0).reshape(lead + (width,))


def all_gather(values, axis, parts):
    dense = values.reshape(-1, LANES)
    copies = jnp.broadcast_to(dense[None], (parts,) + dense.shape)
    moved = lax.all_to_all(copies, axis, 0, 0, tiled=True)
    lead = values.shape[:-1]
    moved = jnp.moveaxis(moved.reshape((parts,) + values.shape), 0, -2)
    return moved.reshape(lead + (parts * values.shape[-1],))


def body(source_mass, target_mass, tile_list, kernel_tiles):
    width = kernel_tiles.shape[-1]
    tiles = kernel_tiles.reshape(-1, width, width)
    listed = tile_list.reshape(-1, 2)
    row_count = source_mass.shape[0]
    col_count = target_mass.shape[0]
    columns = source_mass.shape[1]
    n_col = width // source_mass.shape[2]
    n_row = width // target_mass.shape[2]
    row_local = listed[:, 0] - lax.axis_index("row") * row_count
    col_local = listed[:, 1] - lax.axis_index("col") * col_count
    row_part = collect(row_local, row_count, tiles.sum(axis=2, dtype=jnp.float32)[:, None, :])[:, 0, :]
    payload = jnp.concatenate([source_mass.reshape(-1), row_part.reshape(-1)]).reshape(-1, LANES)
    copies = jnp.broadcast_to(payload[None], (n_col,) + payload.shape)
    moved = lax.all_to_all(copies, "col", 0, 0, tiled=True).reshape(n_col, -1)
    split = source_mass.size
    mass_full = jnp.moveaxis(moved[:, :split].reshape((n_col,) + source_mass.shape), 0, 2)
    mass_full = mass_full.reshape(row_count, columns, width)
    row_full = moved[:, split:].reshape(n_col, row_count, width).sum(axis=0)
    source_full = (mass_full / row_full[:, None, :]).astype(jnp.bfloat16)
    col_sums = reduce_scatter(
        backward_terms(tiles, source_full, row_local, col_local, col_count), "row", n_row
    )
    scale_v = target_mass / col_sums
    for step in range(1, ITERS):
        target_full = all_gather(scale_v.astype(jnp.bfloat16), "row", n_row)
        row_sums = reduce_scatter(
            forward_terms(tiles, target_full, col_local, row_local, row_count), "col", n_col
        )
        scale_u = source_mass / row_sums
        source_full = all_gather(scale_u.astype(jnp.bfloat16), "col", n_col)
        col_sums = reduce_scatter(
            backward_terms(tiles, source_full, row_local, col_local, col_count), "row", n_row
        )
        scale_v = target_mass / col_sums
    log_u = jnp.log(scale_u)
    log_v = jnp.log(scale_v)
    return (log_u, log_v)


def solution(mesh):
    placed = (
        P("row", None, "col"),
        P("col", None, "row"),
        P("row", "col", None, None),
        P("row", "col", None, None, None),
    )
    return jax.shard_map(
        body,
        mesh=mesh,
        in_specs=placed,
        out_specs=(P("row", None, "col"), P("col", None, "row")),
        check_vma=False,
    )
```

```python
import jax
import jax.numpy as jnp
from jax import lax
from jax.sharding import PartitionSpec as P

ITERS = 2
AR1_TWO_ROUNDS = False
FWD_TPC = False
BWD_JS = True


def collect(selector, count, values):
    onehot = (selector[None, :] == jnp.arange(count, dtype=jnp.int32)[:, None]).astype(jnp.float32)
    return jnp.einsum("rt,tcp->rcp", onehot, values, precision=lax.Precision.HIGHEST)


def forward_terms(tiles, target_full, col_local, row_local, count):
    picked = target_full[col_local]
    if FWD_TPC:
        products = jnp.einsum("tcq,tpq->tpc", picked, tiles, preferred_element_type=jnp.float32)
        onehot = (row_local[None, :] == jnp.arange(count, dtype=jnp.int32)[:, None]).astype(jnp.float32)
        return jnp.einsum("rt,tpc->rcp", onehot, products, precision=lax.Precision.HIGHEST)
    products = jnp.einsum("tcq,tpq->tcp", picked, tiles, preferred_element_type=jnp.float32)
    return collect(row_local, count, products)


def backward_terms(tiles, source_full, row_local, col_local, count):
    if BWD_JS:
        picked = source_full[:, row_local]
        parts = picked.shape[0]
        split_tiles = tiles.reshape(tiles.shape[0], parts, -1, tiles.shape[2])
        products = jnp.einsum("jtcs,tjsq->tcq", picked, split_tiles, preferred_element_type=jnp.float32)
        return collect(col_local, count, products)
    picked = source_full[row_local]
    products = jnp.einsum("tcp,tpq->tcq", picked, tiles, preferred_element_type=jnp.float32)
    return collect(col_local, count, products)


LANES = 128


def reduce_scatter(values, axis, parts):
    lead = values.shape[:-1]
    width = values.shape[-1] // parts
    split = jnp.moveaxis(values.reshape(lead + (parts, width)), -2, 0)
    dense = split.reshape(parts, -1, LANES)
    moved = lax.all_to_all(dense, axis, 0, 0, tiled=True)
    return moved.sum(axis=0).reshape(lead + (width,))


def all_gather_parts(values, axis, parts):
    dense = values.reshape(-1, LANES)
    copies = jnp.broadcast_to(dense[None], (parts,) + dense.shape)
    moved = lax.all_to_all(copies, axis, 0, 0, tiled=True)
    return moved.reshape((parts,) + values.shape)


def all_gather(values, axis, parts):
    dense = values.reshape(-1, LANES)
    copies = jnp.broadcast_to(dense[None], (parts,) + dense.shape)
    moved = lax.all_to_all(copies, axis, 0, 0, tiled=True)
    lead = values.shape[:-1]
    moved = jnp.moveaxis(moved.reshape((parts,) + values.shape), 0, -2)
    return moved.reshape(lead + (parts * values.shape[-1],))


def body(source_mass, target_mass, tile_list, kernel_tiles):
    width = kernel_tiles.shape[-1]
    tiles = kernel_tiles.reshape(-1, width, width)
    listed = tile_list.reshape(-1, 2)
    row_count = source_mass.shape[0]
    col_count = target_mass.shape[0]
    columns = source_mass.shape[1]
    n_col = width // source_mass.shape[2]
    n_row = width // target_mass.shape[2]
    row_local = listed[:, 0] - lax.axis_index("row") * row_count
    col_local = listed[:, 1] - lax.axis_index("col") * col_count
    row_part = collect(row_local, row_count, tiles.sum(axis=2, dtype=jnp.float32)[:, None, :])[:, 0, :]
    if AR1_TWO_ROUNDS:
        row_own = reduce_scatter(row_part, "col", n_col)
        scale_1 = source_mass / row_own[:, None, :]
        if BWD_JS:
            source_full = all_gather_parts(scale_1.astype(jnp.bfloat16), "col", n_col)
        else:
            source_full = all_gather(scale_1.astype(jnp.bfloat16), "col", n_col)
    else:
        payload = jnp.concatenate([source_mass.reshape(-1), row_part.reshape(-1)]).reshape(-1, LANES)
        copies = jnp.broadcast_to(payload[None], (n_col,) + payload.shape)
        moved = lax.all_to_all(copies, "col", 0, 0, tiled=True).reshape(n_col, -1)
        split = source_mass.size
        mass_parts = moved[:, :split].reshape((n_col,) + source_mass.shape)
        row_full = moved[:, split:].reshape(n_col, row_count, width).sum(axis=0)
        if BWD_JS:
            row_parts = jnp.moveaxis(row_full.reshape(row_count, n_col, -1), 1, 0)
            source_full = (mass_parts / row_parts[:, :, None, :]).astype(jnp.bfloat16)
        else:
            mass_full = jnp.moveaxis(mass_parts, 0, 2).reshape(row_count, columns, width)
            source_full = (mass_full / row_full[:, None, :]).astype(jnp.bfloat16)
    col_sums = reduce_scatter(
        backward_terms(tiles, source_full, row_local, col_local, col_count), "row", n_row
    )
    scale_v = target_mass / col_sums
    for step in range(1, ITERS):
        target_full = all_gather(scale_v.astype(jnp.bfloat16), "row", n_row)
        row_sums = reduce_scatter(
            forward_terms(tiles, target_full, col_local, row_local, row_count), "col", n_col
        )
        scale_u = source_mass / row_sums
        if BWD_JS:
            source_full = all_gather_parts(scale_u.astype(jnp.bfloat16), "col", n_col)
        else:
            source_full = all_gather(scale_u.astype(jnp.bfloat16), "col", n_col)
        col_sums = reduce_scatter(
            backward_terms(tiles, source_full, row_local, col_local, col_count), "row", n_row
        )
        scale_v = target_mass / col_sums
    log_u = jnp.log(scale_u)
    log_v = jnp.log(scale_v)
    return (log_u, log_v)


def solution(mesh):
    placed = (
        P("row", None, "col"),
        P("col", None, "row"),
        P("row", "col", None, None),
        P("row", "col", None, None, None),
    )
    return jax.shard_map(
        body,
        mesh=mesh,
        in_specs=placed,
        out_specs=(P("row", None, "col"), P("col", None, "row")),
        check_vma=False,
    )
```

```python
import jax
import jax.numpy as jnp
from jax import lax
from jax.sharding import PartitionSpec as P

ITERS = 2
AR1_TWO_ROUNDS = False
FWD_TPC = False
BWD_JS = True
MASS_APART = False
ONEHOT_PICK = True
FWD_T = False


def collect(selector, count, values):
    onehot = (selector[None, :] == jnp.arange(count, dtype=jnp.int32)[:, None]).astype(jnp.float32)
    return jnp.einsum("rt,tcp->rcp", onehot, values, precision=lax.Precision.HIGHEST)


def pick(values, selector, axis):
    if not ONEHOT_PICK:
        return values[selector] if axis == 0 else values[:, selector]
    onehot = (selector[:, None] == jnp.arange(values.shape[axis], dtype=jnp.int32)[None, :]).astype(values.dtype)
    moved = jnp.moveaxis(values, axis, 0)
    chosen = jnp.tensordot(onehot, moved, axes=1, preferred_element_type=jnp.float32).astype(values.dtype)
    return jnp.moveaxis(chosen, 0, axis)


def forward_terms_t(tiles_t, target_parts, col_local, row_local, count):
    picked = pick(target_parts, col_local, 1)
    parts = picked.shape[0]
    split_tiles = tiles_t.reshape(tiles_t.shape[0], parts, -1, tiles_t.shape[2])
    products = jnp.einsum("itcs,tisp->tcp", picked, split_tiles, preferred_element_type=jnp.float32)
    return collect(row_local, count, products)


def forward_terms(tiles, target_full, col_local, row_local, count):
    picked = pick(target_full, col_local, 0)
    if FWD_TPC:
        products = jnp.einsum("tcq,tpq->tpc", picked, tiles, preferred_element_type=jnp.float32)
        onehot = (row_local[None, :] == jnp.arange(count, dtype=jnp.int32)[:, None]).astype(jnp.float32)
        return jnp.einsum("rt,tpc->rcp", onehot, products, precision=lax.Precision.HIGHEST)
    products = jnp.einsum("tcq,tpq->tcp", picked, tiles, preferred_element_type=jnp.float32)
    return collect(row_local, count, products)


def backward_terms(tiles, source_full, row_local, col_local, count):
    if BWD_JS:
        picked = pick(source_full, row_local, 1)
        parts = picked.shape[0]
        split_tiles = tiles.reshape(tiles.shape[0], parts, -1, tiles.shape[2])
        products = jnp.einsum("jtcs,tjsq->tcq", picked, split_tiles, preferred_element_type=jnp.float32)
        return collect(col_local, count, products)
    picked = source_full[row_local]
    products = jnp.einsum("tcp,tpq->tcq", picked, tiles, preferred_element_type=jnp.float32)
    return collect(col_local, count, products)


LANES = 128


def reduce_scatter(values, axis, parts):
    lead = values.shape[:-1]
    width = values.shape[-1] // parts
    split = jnp.moveaxis(values.reshape(lead + (parts, width)), -2, 0)
    dense = split.reshape(parts, -1, LANES)
    moved = lax.all_to_all(dense, axis, 0, 0, tiled=True)
    return moved.sum(axis=0).reshape(lead + (width,))


def all_gather_parts(values, axis, parts):
    dense = values.reshape(-1, LANES)
    copies = jnp.broadcast_to(dense[None], (parts,) + dense.shape)
    moved = lax.all_to_all(copies, axis, 0, 0, tiled=True)
    return moved.reshape((parts,) + values.shape)


def all_gather(values, axis, parts):
    dense = values.reshape(-1, LANES)
    copies = jnp.broadcast_to(dense[None], (parts,) + dense.shape)
    moved = lax.all_to_all(copies, axis, 0, 0, tiled=True)
    lead = values.shape[:-1]
    moved = jnp.moveaxis(moved.reshape((parts,) + values.shape), 0, -2)
    return moved.reshape(lead + (parts * values.shape[-1],))


def body(source_mass, target_mass, tile_list, kernel_tiles):
    width = kernel_tiles.shape[-1]
    tiles = kernel_tiles.reshape(-1, width, width)
    listed = tile_list.reshape(-1, 2)
    row_count = source_mass.shape[0]
    col_count = target_mass.shape[0]
    columns = source_mass.shape[1]
    n_col = width // source_mass.shape[2]
    n_row = width // target_mass.shape[2]
    row_local = listed[:, 0] - lax.axis_index("row") * row_count
    col_local = listed[:, 1] - lax.axis_index("col") * col_count
    row_part = collect(row_local, row_count, tiles.sum(axis=2, dtype=jnp.float32)[:, None, :])[:, 0, :]
    if AR1_TWO_ROUNDS:
        row_own = reduce_scatter(row_part, "col", n_col)
        scale_1 = source_mass / row_own[:, None, :]
        if BWD_JS:
            source_full = all_gather_parts(scale_1.astype(jnp.bfloat16), "col", n_col)
        else:
            source_full = all_gather(scale_1.astype(jnp.bfloat16), "col", n_col)
    else:
        if MASS_APART:
            mass_parts = all_gather_parts(source_mass, "col", n_col)
            row_full = all_gather_parts(row_part, "col", n_col).sum(axis=0)
        else:
            payload = jnp.concatenate([source_mass.reshape(-1), row_part.reshape(-1)]).reshape(-1, LANES)
            copies = jnp.broadcast_to(payload[None], (n_col,) + payload.shape)
            moved = lax.all_to_all(copies, "col", 0, 0, tiled=True).reshape(n_col, -1)
            split = source_mass.size
            mass_parts = moved[:, :split].reshape((n_col,) + source_mass.shape)
            row_full = moved[:, split:].reshape(n_col, row_count, width).sum(axis=0)
        if BWD_JS:
            row_parts = jnp.moveaxis(row_full.reshape(row_count, n_col, -1), 1, 0)
            source_full = (mass_parts / row_parts[:, :, None, :]).astype(jnp.bfloat16)
        else:
            mass_full = jnp.moveaxis(mass_parts, 0, 2).reshape(row_count, columns, width)
            source_full = (mass_full / row_full[:, None, :]).astype(jnp.bfloat16)
    col_sums = reduce_scatter(
        backward_terms(tiles, source_full, row_local, col_local, col_count), "row", n_row
    )
    scale_v = target_mass / col_sums
    if FWD_T:
        tiles_t = lax.optimization_barrier(jnp.swapaxes(tiles, 1, 2))
    for step in range(1, ITERS):
        if FWD_T:
            target_parts = all_gather_parts(scale_v.astype(jnp.bfloat16), "row", n_row)
            terms = forward_terms_t(tiles_t, target_parts, col_local, row_local, row_count)
        else:
            target_full = all_gather(scale_v.astype(jnp.bfloat16), "row", n_row)
            terms = forward_terms(tiles, target_full, col_local, row_local, row_count)
        row_sums = reduce_scatter(terms, "col", n_col)
        scale_u = source_mass / row_sums
        if BWD_JS:
            source_full = all_gather_parts(scale_u.astype(jnp.bfloat16), "col", n_col)
        else:
            source_full = all_gather(scale_u.astype(jnp.bfloat16), "col", n_col)
        col_sums = reduce_scatter(
            backward_terms(tiles, source_full, row_local, col_local, col_count), "row", n_row
        )
        scale_v = target_mass / col_sums
    log_u = jnp.log(scale_u)
    log_v = jnp.log(scale_v)
    return (log_u, log_v)


def solution(mesh):
    placed = (
        P("row", None, "col"),
        P("col", None, "row"),
        P("row", "col", None, None),
        P("row", "col", None, None, None),
    )
    return jax.shard_map(
        body,
        mesh=mesh,
        in_specs=placed,
        out_specs=(P("row", None, "col"), P("col", None, "row")),
        check_vma=False,
    )
```

```python
import jax
import jax.numpy as jnp
from jax import lax
from jax.sharding import PartitionSpec as P

ITERS = 2
LANES = 128


def collect(selector, count, values):
    onehot = (selector[None, :] == jnp.arange(count, dtype=jnp.int32)[:, None]).astype(jnp.float32)
    return jnp.einsum("rt,tcp->rcp", onehot, values, precision=lax.Precision.HIGHEST)


def pick(values, selector, axis):
    onehot = (selector[:, None] == jnp.arange(values.shape[axis], dtype=jnp.int32)[None, :]).astype(values.dtype)
    moved = jnp.moveaxis(values, axis, 0)
    chosen = jnp.tensordot(onehot, moved, axes=1, preferred_element_type=jnp.float32).astype(values.dtype)
    return jnp.moveaxis(chosen, 0, axis)


def forward_terms(tiles, target_full, col_local, row_local, count):
    picked = pick(target_full, col_local, 0)
    products = jnp.einsum("tcq,tpq->tcp", picked, tiles, preferred_element_type=jnp.float32)
    return collect(row_local, count, products)


def backward_terms(tiles, source_parts, row_local, col_local, count):
    picked = pick(source_parts, row_local, 1)
    parts = picked.shape[0]
    split_tiles = tiles.reshape(tiles.shape[0], parts, -1, tiles.shape[2])
    products = jnp.einsum("jtcs,tjsq->tcq", picked, split_tiles, preferred_element_type=jnp.float32)
    return collect(col_local, count, products)


def reduce_scatter(values, axis, parts):
    lead = values.shape[:-1]
    width = values.shape[-1] // parts
    split = jnp.moveaxis(values.reshape(lead + (parts, width)), -2, 0)
    dense = split.reshape(parts, -1, LANES)
    moved = lax.all_to_all(dense, axis, 0, 0, tiled=True)
    return moved.sum(axis=0).reshape(lead + (width,))


def all_gather_parts(values, axis, parts):
    dense = values.reshape(-1, LANES)
    copies = jnp.broadcast_to(dense[None], (parts,) + dense.shape)
    moved = lax.all_to_all(copies, axis, 0, 0, tiled=True)
    return moved.reshape((parts,) + values.shape)


def all_gather(values, axis, parts):
    moved = jnp.moveaxis(all_gather_parts(values, axis, parts), 0, -2)
    return moved.reshape(values.shape[:-1] + (parts * values.shape[-1],))


def body(source_mass, target_mass, tile_list, kernel_tiles):
    width = kernel_tiles.shape[-1]
    tiles = kernel_tiles.reshape(-1, width, width)
    listed = tile_list.reshape(-1, 2)
    row_count = source_mass.shape[0]
    col_count = target_mass.shape[0]
    n_col = width // source_mass.shape[2]
    n_row = width // target_mass.shape[2]
    row_local = listed[:, 0] - lax.axis_index("row") * row_count
    col_local = listed[:, 1] - lax.axis_index("col") * col_count
    row_part = collect(row_local, row_count, tiles.sum(axis=2, dtype=jnp.float32)[:, None, :])[:, 0, :]
    payload = jnp.concatenate([source_mass.reshape(-1), row_part.reshape(-1)]).reshape(-1, LANES)
    copies = jnp.broadcast_to(payload[None], (n_col,) + payload.shape)
    moved = lax.all_to_all(copies, "col", 0, 0, tiled=True).reshape(n_col, -1)
    split = source_mass.size
    mass_parts = moved[:, :split].reshape((n_col,) + source_mass.shape)
    row_full = moved[:, split:].reshape(n_col, row_count, width).sum(axis=0)
    row_parts = jnp.moveaxis(row_full.reshape(row_count, n_col, -1), 1, 0)
    source_parts = (mass_parts / row_parts[:, :, None, :]).astype(jnp.bfloat16)
    col_sums = reduce_scatter(
        backward_terms(tiles, source_parts, row_local, col_local, col_count), "row", n_row
    )
    scale_v = target_mass / col_sums
    for step in range(1, ITERS):
        target_full = all_gather(scale_v.astype(jnp.bfloat16), "row", n_row)
        row_sums = reduce_scatter(
            forward_terms(tiles, target_full, col_local, row_local, row_count), "col", n_col
        )
        scale_u = source_mass / row_sums
        source_parts = all_gather_parts(scale_u.astype(jnp.bfloat16), "col", n_col)
        col_sums = reduce_scatter(
            backward_terms(tiles, source_parts, row_local, col_local, col_count), "row", n_row
        )
        scale_v = target_mass / col_sums
    log_u = jnp.log(scale_u)
    log_v = jnp.log(scale_v)
    return (log_u, log_v)


def solution(mesh):
    placed = (
        P("row", None, "col"),
        P("col", None, "row"),
        P("row", "col", None, None),
        P("row", "col", None, None, None),
    )
    return jax.shard_map(
        body,
        mesh=mesh,
        in_specs=placed,
        out_specs=(P("row", None, "col"), P("col", None, "row")),
        check_vma=False,
    )
```

```python
import jax
import jax.numpy as jnp
from jax import lax
from jax.sharding import PartitionSpec as P

ITERS = 2
LANES = 128


def collect(selector, count, values):
    onehot = (selector[None, :] == jnp.arange(count, dtype=jnp.int32)[:, None]).astype(jnp.float32)
    return jnp.einsum("rt,tcp->rcp", onehot, values, precision=lax.Precision.HIGH)


def pick(values, selector, axis):
    onehot = (selector[:, None] == jnp.arange(values.shape[axis], dtype=jnp.int32)[None, :]).astype(values.dtype)
    moved = jnp.moveaxis(values, axis, 0)
    chosen = jnp.tensordot(onehot, moved, axes=1, preferred_element_type=jnp.float32).astype(values.dtype)
    return jnp.moveaxis(chosen, 0, axis)


def forward_terms(tiles, target_full, col_local, row_local, count):
    picked = pick(target_full, col_local, 0)
    products = jnp.einsum("tcq,tpq->tcp", picked, tiles, preferred_element_type=jnp.float32)
    return collect(row_local, count, products)


def backward_terms(tiles, source_parts, row_local, col_local, count):
    picked = pick(source_parts, row_local, 1)
    parts = picked.shape[0]
    split_tiles = tiles.reshape(tiles.shape[0], parts, -1, tiles.shape[2])
    products = jnp.einsum("jtcs,tjsq->tcq", picked, split_tiles, preferred_element_type=jnp.float32)
    return collect(col_local, count, products)


def reduce_scatter(values, axis, parts):
    lead = values.shape[:-1]
    width = values.shape[-1] // parts
    split = jnp.moveaxis(values.reshape(lead + (parts, width)), -2, 0)
    dense = split.reshape(parts, -1, LANES)
    moved = lax.all_to_all(dense, axis, 0, 0, tiled=True)
    return moved.sum(axis=0).reshape(lead + (width,))


def all_gather_parts(values, axis, parts):
    dense = values.reshape(-1, LANES)
    copies = jnp.broadcast_to(dense[None], (parts,) + dense.shape)
    moved = lax.all_to_all(copies, axis, 0, 0, tiled=True)
    return moved.reshape((parts,) + values.shape)


def all_gather(values, axis, parts):
    moved = jnp.moveaxis(all_gather_parts(values, axis, parts), 0, -2)
    return moved.reshape(values.shape[:-1] + (parts * values.shape[-1],))


def body(source_mass, target_mass, tile_list, kernel_tiles):
    width = kernel_tiles.shape[-1]
    tiles = kernel_tiles.reshape(-1, width, width)
    listed = tile_list.reshape(-1, 2)
    row_count = source_mass.shape[0]
    col_count = target_mass.shape[0]
    n_col = width // source_mass.shape[2]
    n_row = width // target_mass.shape[2]
    row_local = listed[:, 0] - lax.axis_index("row") * row_count
    col_local = listed[:, 1] - lax.axis_index("col") * col_count
    row_part = collect(row_local, row_count, tiles.sum(axis=2, dtype=jnp.float32)[:, None, :])[:, 0, :]
    payload = jnp.concatenate([source_mass.reshape(-1), row_part.reshape(-1)]).reshape(-1, LANES)
    copies = jnp.broadcast_to(payload[None], (n_col,) + payload.shape)
    moved = lax.all_to_all(copies, "col", 0, 0, tiled=True).reshape(n_col, -1)
    split = source_mass.size
    mass_parts = moved[:, :split].reshape((n_col,) + source_mass.shape)
    row_full = moved[:, split:].reshape(n_col, row_count, width).sum(axis=0)
    row_parts = jnp.moveaxis(row_full.reshape(row_count, n_col, -1), 1, 0)
    source_parts = (mass_parts / row_parts[:, :, None, :]).astype(jnp.bfloat16)
    col_sums = reduce_scatter(
        backward_terms(tiles, source_parts, row_local, col_local, col_count), "row", n_row
    )
    scale_v = target_mass / col_sums
    for step in range(1, ITERS):
        target_full = all_gather(scale_v.astype(jnp.bfloat16), "row", n_row)
        row_sums = reduce_scatter(
            forward_terms(tiles, target_full, col_local, row_local, row_count), "col", n_col
        )
        scale_u = source_mass / row_sums
        source_parts = all_gather_parts(scale_u.astype(jnp.bfloat16), "col", n_col)
        col_sums = reduce_scatter(
            backward_terms(tiles, source_parts, row_local, col_local, col_count), "row", n_row
        )
        scale_v = target_mass / col_sums
    log_u = jnp.log(scale_u)
    log_v = jnp.log(scale_v)
    return (log_u, log_v)


def solution(mesh):
    placed = (
        P("row", None, "col"),
        P("col", None, "row"),
        P("row", "col", None, None),
        P("row", "col", None, None, None),
    )
    return jax.shard_map(
        body,
        mesh=mesh,
        in_specs=placed,
        out_specs=(P("row", None, "col"), P("col", None, "row")),
        check_vma=False,
    )
```
